32 devices in a mesh: gx: 4 (over z), gy: 4 (over y, x), dp: 2 (over core).
Axes of the slice: x: 2, y: 2, z: 4, core: 2. Of those that a mesh axis runs over, the one named last changes fastest.
Arguments:
- volumes: bfloat16 [6, 32, 32, 32, 128], P('dp', 'gx', 'gy'), may hold values from -6 to 6
- weight_one: bfloat16 [27, 128, 128], replicated, may hold values from -0.109375 to 0.109375
- weight_two: bfloat16 [27, 128, 128], replicated, may hold values from -0.109375 to 0.109375
- cotangent: bfloat16 [6, 32, 32, 32, 128], P('dp', 'gx', 'gy'), may hold values from -0.013671875 to 0.013671875
Outputs:
- features: bfloat16 [6, 32, 32, 32, 128], P('dp', 'gx', 'gy')
- grad_one: float32 [27, 128, 128], replicated
- grad_two: float32 [27, 128, 128], replicated
The draws below stay inside these ranges and needn't reach their ends.
All inputs are finite; a program needn't handle non-finite values.
Results may differ from the reference program's by a relative error of at most 0.0054.
Values may be sent and summed in bfloat16 or wider, within the bound.
No kernel may reach another device: no remote copies, remote signals or barrier semaphores. Data moves between devices by JAX's collectives and lax.ppermute only.
A program may use at most 128 MiB of HBM per device.

```python
import jax
import jax.numpy as jnp
from jax import lax

C = 128
CUBE = 32
CUBES = 6


def levels(own_key, dims, pieces, low, top_value):
    gain = 1.0
    for position, parts in pieces:
        draws = jax.random.uniform(jax.random.fold_in(jax.random.fold_in(own_key, 6), position), (parts,), jnp.float32, low / len(pieces), top_value / len(pieces))
        gain = gain * jnp.repeat(jnp.exp(draws), dims[position] // parts).reshape((-1,) + (1,) * (len(dims) - 1 - position))
    return gain


def centred(key, extent, scale, most, cuts=(), kind=jnp.bfloat16):
    gain = levels(key, extent, cuts, -0.22, 0.18) if cuts else 1.0
    entries = jax.random.normal(key, extent, jnp.float32) * scale * gain
    return jnp.minimum(jnp.maximum(entries, -most), most).astype(kind)


def setup_inputs(seed: int = 0) -> dict:
    key_of = jax.random.split(jax.random.key(seed), 5)
    volumes = centred(key_of[0], (CUBES, CUBE, CUBE, CUBE, C), 1.0, 6.0, ((0, 2), (1, 4), (2, 4)))
    weight_one = centred(key_of[1], (27, C, C), (27 * C) ** -0.5, 0.109375)
    weight_two = centred(key_of[2], (27, C, C), (27 * C) ** -0.5, 0.109375)
    cotangent = centred(key_of[3], (CUBES, CUBE, CUBE, CUBE, C), (CUBES * CUBE * CUBE * CUBE) ** -0.5, 0.013671875, ((0, 2), (1, 4), (2, 4)))
    return {"volumes": volumes, "weight_one": weight_one, "weight_two": weight_two, "cotangent": cotangent}


def conv_columns(field):
    padded = jnp.pad(field, ((1, 1), (1, 1), (1, 1), (0, 0)))
    side_x, side_y, side_z, depth = field.shape
    slices = []
    for shift_a in range(3):
        for shift_b in range(3):
            for shift_c in range(3):
                slices.append(padded[shift_a:shift_a + side_x, shift_b:shift_b + side_y, shift_c:shift_c + side_z, :])
    return jnp.concatenate(slices, axis=-1).reshape(side_x * side_y * side_z, 27 * depth)


def matmul(left, right):
    return jnp.dot(left.astype(jnp.float32), right.astype(jnp.float32), precision=lax.Precision.HIGHEST)


def tmatmul(left, right):
    return jnp.dot(left.astype(jnp.float32).T, right.astype(jnp.float32), precision=lax.Precision.HIGHEST)


def swish_slope(value):
    sigma = jax.nn.sigmoid(value)
    return sigma * (1.0 + value * (1.0 - sigma))


def reference(volumes, weight_one, weight_two, cotangent):
    depth = weight_one.shape[1]
    flat_one = weight_one.reshape(27 * depth, depth)
    flat_two = weight_two.reshape(27 * depth, depth)
    flipped = jnp.transpose(weight_two[::-1], (0, 2, 1)).reshape(27 * depth, depth)
    layout = volumes.shape[1:]

    def one_cube(totals, inputs):
        volume, upstream = inputs
        columns_in = conv_columns(volume)
        act_one = matmul(columns_in, flat_one)
        hidden = jax.nn.silu(act_one).astype(jnp.bfloat16)
        columns_hid = conv_columns(hidden.reshape(layout))
        act_two = matmul(columns_hid, flat_two)
        features = jax.nn.silu(act_two).astype(jnp.bfloat16)
        upstream_rows = upstream.reshape(-1, depth).astype(jnp.float32)
        delta_two = (upstream_rows * swish_slope(act_two)).astype(jnp.bfloat16)
        back_grad = matmul(conv_columns(delta_two.reshape(layout)), flipped)
        delta_one = (back_grad * swish_slope(act_one)).astype(jnp.bfloat16)
        sum_two = totals[1] + tmatmul(columns_hid, delta_two)
        sum_one = totals[0] + tmatmul(columns_in, delta_one)
        return (sum_one, sum_two), features.reshape(layout)

    zeros = jnp.zeros((27 * depth, depth), jnp.float32)
    totals, features = lax.scan(one_cube, (zeros, zeros), (volumes, cotangent))
    return features, totals[0].reshape(27, depth, depth), totals[1].reshape(27, depth, depth)
```

```python
import jax
import jax.numpy as jnp
from jax import lax
from jax.sharding import PartitionSpec as P


def extended(cells, sides, width):
    for axis, dim in sides:
        count = lax.axis_size(axis)
        ends = count - 1
        head = lax.slice_in_dim(cells, 0, width, axis=dim)
        tail = lax.slice_in_dim(cells, cells.shape[dim] - width, cells.shape[dim], axis=dim)
        cells = jnp.concatenate(
            [
                lax.ppermute(tail, axis, [(i, (i + 1) % count) for i in range(ends)]),
                cells,
                lax.ppermute(head, axis, [((i + 1) % count, i) for i in range(ends)]),
            ],
            axis=dim,
        )
    return cells


def conv_block(padded, kernel):
    depth = kernel.shape[1]
    cube_kernel = kernel.reshape(3, 3, 3, depth, depth)
    return lax.conv_general_dilated(
        padded,
        cube_kernel,
        (1, 1, 1),
        ((0, 0), (0, 0), (1, 1)),
        dimension_numbers=("NDHWC", "DHWIO", "NDHWC"),
        preferred_element_type=jnp.float32,
    )


def kernel_grad(padded, delta_field):
    depth = delta_field.shape[4]
    result = lax.conv_general_dilated(
        padded,
        delta_field,
        (1, 1, 1),
        ((0, 0), (0, 0), (1, 1)),
        dimension_numbers=("CDHWN", "IDHWO", "DHWNC"),
        preferred_element_type=jnp.float32,
    )
    return result.reshape(27 * depth, depth)


def swish_slope(value):
    sigma = jax.nn.sigmoid(value)
    return sigma * (1.0 + value * (1.0 - sigma))


def tree_sum(value, axes):
    sizes = [lax.axis_size(axis) for axis in axes]
    if any(n & (n - 1) for n in sizes):
        return lax.psum(value, axes)
    steps = []
    total = 1
    for axis, n in zip(axes, sizes):
        bit = n // 2
        while bit >= 1:
            steps.append((axis, n, bit))
            bit //= 2
        total *= n
    flat = value.reshape(-1)
    unit = total * 8 * 128
    size = flat.shape[0]
    rows = jnp.pad(flat, (0, -(-size // unit) * unit - size)).reshape(-1, 128)
    sides = []
    for axis, n, bit in steps:
        side = (lax.axis_index(axis) // bit) % 2
        half = rows.shape[0] // 2
        pairs = [(i, i ^ bit) for i in range(n)]
        keep = lax.dynamic_slice_in_dim(rows, side * half, half, 0)
        send = lax.dynamic_slice_in_dim(rows, (1 - side) * half, half, 0)
        rows = keep + lax.ppermute(send, axis, pairs)
        sides.append(side)
    for (axis, n, bit), side in zip(reversed(steps), reversed(sides)):
        pairs = [(i, i ^ bit) for i in range(n)]
        other = lax.ppermute(rows, axis, pairs)
        low = jnp.where(side == 0, rows, other)
        high = jnp.where(side == 0, other, rows)
        rows = jnp.concatenate([low, high], 0)
    return rows.reshape(-1)[:size].reshape(value.shape)


def weight_grad(padded, delta_field):
    local_grad = kernel_grad(padded, delta_field)
    return tree_sum(local_grad, ("dp", "gy", "gx"))


def per_device(volumes, weight_one, weight_two, cotangent):
    layout = volumes.shape
    depth = layout[4]
    flipped = jnp.transpose(weight_two[::-1], (0, 2, 1))
    rim_input = extended(volumes, (("gx", 1), ("gy", 2)), 1)
    act_one = lax.optimization_barrier(conv_block(rim_input, weight_one))
    hidden = jax.nn.silu(act_one).astype(jnp.bfloat16)
    rim_hidden = extended(hidden, (("gx", 1), ("gy", 2)), 1)
    act_two = conv_block(rim_hidden, weight_two)
    features = jax.nn.silu(act_two).astype(jnp.bfloat16)
    delta_two = (cotangent.astype(jnp.float32) * swish_slope(act_two)).astype(jnp.bfloat16)
    grad_two = weight_grad(rim_hidden, delta_two)
    rim_delta = extended(delta_two, (("gx", 1), ("gy", 2)), 1)
    back_grad = conv_block(rim_delta, flipped)
    delta_one = (back_grad * swish_slope(act_one)).astype(jnp.bfloat16)
    grad_one = weight_grad(rim_input, delta_one)
    return (features, grad_one.reshape(27, depth, depth), grad_two.reshape(27, depth, depth))


def solution(mesh):
    in_specs = (P("dp", "gx", "gy", None, None), P(), P(), P("dp", "gx", "gy", None, None))
    out_specs = (P("dp", "gx", "gy", None, None), P(), P())
    return jax.shard_map(
        per_device, mesh=mesh, in_specs=in_specs, out_specs=out_specs, check_vma=False
    )
```

```python
import jax
import jax.numpy as jnp
from jax import lax
from jax.sharding import PartitionSpec as P


def neighbour_piece(cells, dx, dy):
    rows = cells.shape[1]
    cols = cells.shape[2]
    piece = cells
    if dx:
        start = rows - 1 if dx < 0 else 0
        piece = lax.slice_in_dim(piece, start, start + 1, axis=1)
    if dy:
        start = cols - 1 if dy < 0 else 0
        piece = lax.slice_in_dim(piece, start, start + 1, axis=2)
    nx = lax.axis_size("gx")
    ny = lax.axis_size("gy")
    pairs = []
    for i in range(nx):
        for j in range(ny):
            si, sj = i + dx, j + dy
            if 0 <= si < nx and 0 <= sj < ny:
                if dx and dy:
                    pairs.append((si * ny + sj, i * ny + j))
                elif dx:
                    if j == 0:
                        pairs.append((si, i))
                else:
                    if i == 0:
                        pairs.append((sj, j))
    if dx and dy:
        axis = ("gx", "gy")
    elif dx:
        axis = "gx"
    else:
        axis = "gy"
    return lax.ppermute(piece, axis, pairs)


def extended(cells):
    got = {}
    for dx in (-1, 0, 1):
        for dy in (-1, 0, 1):
            if dx or dy:
                got[dx, dy] = neighbour_piece(cells, dx, dy)
    got[0, 0] = cells
    bands = [jnp.concatenate([got[dx, dy] for dy in (-1, 0, 1)], axis=2) for dx in (-1, 0, 1)]
    return jnp.concatenate(bands, axis=1)


def conv_block(padded, kernel):
    depth = kernel.shape[1]
    cube_kernel = kernel.reshape(3, 3, 3, depth, depth)
    return lax.conv_general_dilated(
        padded,
        cube_kernel,
        (1, 1, 1),
        ((0, 0), (0, 0), (1, 1)),
        dimension_numbers=("NDHWC", "DHWIO", "NDHWC"),
        preferred_element_type=jnp.float32,
    )


def kernel_grad(padded, delta_field):
    depth = delta_field.shape[4]
    result = lax.conv_general_dilated(
        padded,
        delta_field,
        (1, 1, 1),
        ((0, 0), (0, 0), (1, 1)),
        dimension_numbers=("CDHWN", "IDHWO", "DHWNC"),
        preferred_element_type=jnp.float32,
    )
    return result.reshape(27 * depth, depth)


def swish_slope(value):
    sigma = jax.nn.sigmoid(value)
    return sigma * (1.0 + value * (1.0 - sigma))


def tree_sum(value, axes):
    sizes = [lax.axis_size(axis) for axis in axes]
    if any(n & (n - 1) for n in sizes):
        return lax.psum(value, axes)
    steps = []
    total = 1
    for axis, n in zip(axes, sizes):
        bit = n // 2
        while bit >= 1:
            steps.append((axis, n, bit))
            bit //= 2
        total *= n
    flat = value.reshape(-1)
    unit = total * 8 * 128
    size = flat.shape[0]
    rows = jnp.pad(flat, (0, -(-size // unit) * unit - size)).reshape(-1, 128)
    sides = []
    for axis, n, bit in steps:
        side = (lax.axis_index(axis) // bit) % 2
        half = rows.shape[0] // 2
        pairs = [(i, i ^ bit) for i in range(n)]
        keep = lax.dynamic_slice_in_dim(rows, side * half, half, 0)
        send = lax.dynamic_slice_in_dim(rows, (1 - side) * half, half, 0)
        rows = keep + lax.ppermute(send, axis, pairs)
        sides.append(side)
    for (axis, n, bit), side in zip(reversed(steps), reversed(sides)):
        pairs = [(i, i ^ bit) for i in range(n)]
        other = lax.ppermute(rows, axis, pairs)
        low = jnp.where(side == 0, rows, other)
        high = jnp.where(side == 0, other, rows)
        rows = jnp.concatenate([low, high], 0)
    return rows.reshape(-1)[:size].reshape(value.shape)


def weight_grad(padded, delta_field):
    local_grad = kernel_grad(padded, delta_field)
    return tree_sum(local_grad, ("dp", "gy", "gx"))


def per_device(volumes, weight_one, weight_two, cotangent):
    layout = volumes.shape
    depth = layout[4]
    flipped = jnp.transpose(weight_two[::-1], (0, 2, 1))
    rim_input = extended(volumes)
    act_one = lax.optimization_barrier(conv_block(rim_input, weight_one))
    hidden = jax.nn.silu(act_one).astype(jnp.bfloat16)
    rim_hidden = extended(hidden)
    act_two = conv_block(rim_hidden, weight_two)
    features = jax.nn.silu(act_two).astype(jnp.bfloat16)
    delta_two = (cotangent.astype(jnp.float32) * swish_slope(act_two)).astype(jnp.bfloat16)
    grad_two = weight_grad(rim_hidden, delta_two)
    rim_delta = extended(delta_two)
    back_grad = conv_block(rim_delta, flipped)
    delta_one = (back_grad * swish_slope(act_one)).astype(jnp.bfloat16)
    grad_one = weight_grad(rim_input, delta_one)
    return (features, grad_one.reshape(27, depth, depth), grad_two.reshape(27, depth, depth))


def solution(mesh):
    in_specs = (P("dp", "gx", "gy", None, None), P(), P(), P("dp", "gx", "gy", None, None))
    out_specs = (P("dp", "gx", "gy", None, None), P(), P())
    return jax.shard_map(
        per_device, mesh=mesh, in_specs=in_specs, out_specs=out_specs, check_vma=False
    )
```

```python
import jax
import jax.numpy as jnp
from jax import lax
from jax.sharding import PartitionSpec as P


def extended(cells, sides, width):
    for axis, dim in sides:
        count = lax.axis_size(axis)
        ends = count - 1
        head = lax.slice_in_dim(cells, 0, width, axis=dim)
        tail = lax.slice_in_dim(cells, cells.shape[dim] - width, cells.shape[dim], axis=dim)
        cells = jnp.concatenate(
            [
                lax.ppermute(tail, axis, [(i, (i + 1) % count) for i in range(ends)]),
                cells,
                lax.ppermute(head, axis, [((i + 1) % count, i) for i in range(ends)]),
            ],
            axis=dim,
        )
    return cells


def conv_block(padded, kernel):
    depth = kernel.shape[1]
    cube_kernel = kernel.reshape(3, 3, 3, depth, depth)
    return lax.conv_general_dilated(
        padded,
        cube_kernel,
        (1, 1, 1),
        ((0, 0), (0, 0), (1, 1)),
        dimension_numbers=("NDHWC", "DHWIO", "NDHWC"),
        preferred_element_type=jnp.float32,
    )


def kernel_grad(padded, delta_field):
    depth = delta_field.shape[4]
    result = lax.conv_general_dilated(
        padded,
        delta_field,
        (1, 1, 1),
        ((0, 0), (0, 0), (1, 1)),
        dimension_numbers=("CDHWN", "IDHWO", "DHWNC"),
        preferred_element_type=jnp.float32,
    )
    return result.reshape(27 * depth, depth)


def swish_slope(value):
    sigma = jax.nn.sigmoid(value)
    return sigma * (1.0 + value * (1.0 - sigma))


def tree_sum(value, axes):
    sizes = [lax.axis_size(axis) for axis in axes]
    if any(n & (n - 1) for n in sizes):
        return lax.psum(value, axes)
    steps = []
    total = 1
    for axis, n in zip(axes, sizes):
        bit = n // 2
        while bit >= 1:
            steps.append((axis, n, bit))
            bit //= 2
        total *= n
    flat = value.reshape(-1)
    unit = total * 8 * 128
    size = flat.shape[0]
    rows = jnp.pad(flat, (0, -(-size // unit) * unit - size)).reshape(-1, 128)
    sides = []
    for axis, n, bit in steps:
        side = (lax.axis_index(axis) // bit) % 2
        half = rows.shape[0] // 2
        pairs = [(i, i ^ bit) for i in range(n)]
        keep = lax.dynamic_slice_in_dim(rows, side * half, half, 0)
        send = lax.dynamic_slice_in_dim(rows, (1 - side) * half, half, 0)
        rows = keep + lax.ppermute(send, axis, pairs)
        sides.append(side)
    for (axis, n, bit), side in zip(reversed(steps), reversed(sides)):
        pairs = [(i, i ^ bit) for i in range(n)]
        other = lax.ppermute(rows, axis, pairs)
        low = jnp.where(side == 0, rows, other)
        high = jnp.where(side == 0, other, rows)
        rows = jnp.concatenate([low, high], 0)
    return rows.reshape(-1)[:size].reshape(value.shape)


def weight_grad(padded, delta_field, after=None):
    local_grad = kernel_grad(padded, delta_field)
    if after is not None:
        after, local_grad = lax.optimization_barrier((after, local_grad))
    return after, tree_sum(local_grad, ("dp", "gy", "gx"))


def per_device(volumes, weight_one, weight_two, cotangent):
    layout = volumes.shape
    depth = layout[4]
    flipped = jnp.transpose(weight_two[::-1], (0, 2, 1))
    rim_input = extended(volumes, (("gx", 1), ("gy", 2)), 1)
    act_one = lax.optimization_barrier(conv_block(rim_input, weight_one))
    hidden = jax.nn.silu(act_one).astype(jnp.bfloat16)
    rim_hidden = extended(hidden, (("gx", 1), ("gy", 2)), 1)
    act_two = conv_block(rim_hidden, weight_two)
    features = jax.nn.silu(act_two).astype(jnp.bfloat16)
    delta_two = (cotangent.astype(jnp.float32) * swish_slope(act_two)).astype(jnp.bfloat16)
    _, grad_two = weight_grad(rim_hidden, delta_two)
    rim_delta = extended(delta_two, (("gx", 1), ("gy", 2)), 1)
    back_grad = conv_block(rim_delta, flipped)
    delta_one = (back_grad * swish_slope(act_one)).astype(jnp.bfloat16)
    grad_two, grad_one = weight_grad(rim_input, delta_one, grad_two)
    return (features, grad_one.reshape(27, depth, depth), grad_two.reshape(27, depth, depth))


def solution(mesh):
    in_specs = (P("dp", "gx", "gy", None, None), P(), P(), P("dp", "gx", "gy", None, None))
    out_specs = (P("dp", "gx", "gy", None, None), P(), P())
    return jax.shard_map(
        per_device, mesh=mesh, in_specs=in_specs, out_specs=out_specs, check_vma=False
    )
```

```python
import jax
import jax.numpy as jnp
from jax import lax
from jax.sharding import PartitionSpec as P


def extended(cells, sides, width):
    for axis, dim in sides:
        count = lax.axis_size(axis)
        ends = count - 1
        head = lax.slice_in_dim(cells, 0, width, axis=dim)
        tail = lax.slice_in_dim(cells, cells.shape[dim] - width, cells.shape[dim], axis=dim)
        cells = jnp.concatenate(
            [
                lax.ppermute(tail, axis, [(i, (i + 1) % count) for i in range(ends)]),
                cells,
                lax.ppermute(head, axis, [((i + 1) % count, i) for i in range(ends)]),
            ],
            axis=dim,
        )
    return cells


def conv_block(padded, kernel):
    depth = kernel.shape[1]
    cube_kernel = kernel.reshape(3, 3, 3, depth, depth)
    return lax.conv_general_dilated(
        padded,
        cube_kernel,
        (1, 1, 1),
        ((0, 0), (0, 0), (1, 1)),
        dimension_numbers=("NDHWC", "DHWIO", "NDHWC"),
        preferred_element_type=jnp.float32,
    )


def kernel_grad(padded, delta_field):
    depth = delta_field.shape[4]
    result = lax.conv_general_dilated(
        padded,
        delta_field,
        (1, 1, 1),
        ((0, 0), (0, 0), (1, 1)),
        dimension_numbers=("CDHWN", "IDHWO", "DHWNC"),
        preferred_element_type=jnp.float32,
    )
    return result.reshape(27 * depth, depth)


def swish_slope(value):
    sigma = jax.nn.sigmoid(value)
    return sigma * (1.0 + value * (1.0 - sigma))


def tree_sum(value, axes):
    sizes = [lax.axis_size(axis) for axis in axes]
    if any(n & (n - 1) for n in sizes):
        return lax.psum(value, axes)
    steps = []
    total = 1
    for axis, n in zip(axes, sizes):
        bit = n // 2
        while bit >= 1:
            steps.append((axis, n, bit))
            bit //= 2
        total *= n
    flat = value.reshape(-1)
    unit = total * 8 * 128
    size = flat.shape[0]
    rows = jnp.pad(flat, (0, -(-size // unit) * unit - size)).reshape(-1, 128)
    sides = []
    for axis, n, bit in steps:
        side = (lax.axis_index(axis) // bit) % 2
        half = rows.shape[0] // 2
        pairs = [(i, i ^ bit) for i in range(n)]
        keep = lax.dynamic_slice_in_dim(rows, side * half, half, 0)
        send = lax.dynamic_slice_in_dim(rows, (1 - side) * half, half, 0)
        rows = keep + lax.ppermute(send, axis, pairs)
        sides.append(side)
    rows = rows.astype(jnp.bfloat16)
    for (axis, n, bit), side in zip(reversed(steps), reversed(sides)):
        pairs = [(i, i ^ bit) for i in range(n)]
        other = lax.ppermute(rows, axis, pairs)
        low = jnp.where(side == 0, rows, other)
        high = jnp.where(side == 0, other, rows)
        rows = jnp.concatenate([low, high], 0)
    return rows.reshape(-1)[:size].reshape(value.shape).astype(value.dtype)


def weight_grad(padded, delta_field):
    local_grad = kernel_grad(padded, delta_field)
    return tree_sum(local_grad, ("dp", "gy", "gx"))


def per_device(volumes, weight_one, weight_two, cotangent):
    layout = volumes.shape
    depth = layout[4]
    flipped = jnp.transpose(weight_two[::-1], (0, 2, 1))
    rim_input = extended(volumes, (("gx", 1), ("gy", 2)), 1)
    act_one = lax.optimization_barrier(conv_block(rim_input, weight_one))
    hidden = jax.nn.silu(act_one).astype(jnp.bfloat16)
    rim_hidden = extended(hidden, (("gx", 1), ("gy", 2)), 1)
    act_two = conv_block(rim_hidden, weight_two)
    features = jax.nn.silu(act_two).astype(jnp.bfloat16)
    delta_two = (cotangent.astype(jnp.float32) * swish_slope(act_two)).astype(jnp.bfloat16)
    grad_two = weight_grad(rim_hidden, delta_two)
    rim_delta = extended(delta_two, (("gx", 1), ("gy", 2)), 1)
    back_grad = conv_block(rim_delta, flipped)
    delta_one = (back_grad * swish_slope(act_one)).astype(jnp.bfloat16)
    grad_one = weight_grad(rim_input, delta_one)
    return (features, grad_one.reshape(27, depth, depth), grad_two.reshape(27, depth, depth))


def solution(mesh):
    in_specs = (P("dp", "gx", "gy", None, None), P(), P(), P("dp", "gx", "gy", None, None))
    out_specs = (P("dp", "gx", "gy", None, None), P(), P())
    return jax.shard_map(
        per_device, mesh=mesh, in_specs=in_specs, out_specs=out_specs, check_vma=False
    )
```

```python
import jax
import jax.numpy as jnp
from jax import lax
from jax.sharding import PartitionSpec as P


def extended(cells, sides, width):
    for axis, dim in sides:
        count = lax.axis_size(axis)
        ends = count - 1
        head = lax.slice_in_dim(cells, 0, width, axis=dim)
        tail = lax.slice_in_dim(cells, cells.shape[dim] - width, cells.shape[dim], axis=dim)
        cells = jnp.concatenate(
            [
                lax.ppermute(tail, axis, [(i, (i + 1) % count) for i in range(ends)]),
                cells,
                lax.ppermute(head, axis, [((i + 1) % count, i) for i in range(ends)]),
            ],
            axis=dim,
        )
    return cells


def conv_block(padded, kernel):
    depth = kernel.shape[1]
    cube_kernel = kernel.reshape(3, 3, 3, depth, depth)
    return lax.conv_general_dilated(
        padded,
        cube_kernel,
        (1, 1, 1),
        ((0, 0), (0, 0), (1, 1)),
        dimension_numbers=("NDHWC", "DHWIO", "NDHWC"),
        preferred_element_type=jnp.float32,
    )


def kernel_grad(padded, delta_field):
    depth = delta_field.shape[4]
    result = lax.conv_general_dilated(
        padded,
        delta_field,
        (1, 1, 1),
        ((0, 0), (0, 0), (1, 1)),
        dimension_numbers=("CDHWN", "IDHWO", "DHWNC"),
        preferred_element_type=jnp.float32,
    )
    return result.reshape(27 * depth, depth)


def swish_slope(value):
    sigma = jax.nn.sigmoid(value)
    return sigma * (1.0 + value * (1.0 - sigma))


def tree_sum(value, axes):
    sizes = [lax.axis_size(axis) for axis in axes]
    if any(n & (n - 1) for n in sizes):
        return lax.psum(value, axes)
    steps = []
    total = 1
    for axis, n in zip(axes, sizes):
        bit = 1
        while bit < n:
            steps.append((axis, n, bit))
            bit *= 2
        total *= n
    flat = value.reshape(-1)
    unit = total * 8 * 128
    size = flat.shape[0]
    rows = jnp.pad(flat, (0, -(-size // unit) * unit - size)).reshape(-1, 128)
    sides = []
    for axis, n, bit in steps:
        side = (lax.axis_index(axis) // bit) % 2
        half = rows.shape[0] // 2
        pairs = [(i, i ^ bit) for i in range(n)]
        keep = lax.dynamic_slice_in_dim(rows, side * half, half, 0)
        send = lax.dynamic_slice_in_dim(rows, (1 - side) * half, half, 0)
        rows = keep + lax.ppermute(send, axis, pairs)
        sides.append(side)
    rows = rows.astype(jnp.bfloat16)
    for (axis, n, bit), side in zip(reversed(steps), reversed(sides)):
        pairs = [(i, i ^ bit) for i in range(n)]
        other = lax.ppermute(rows, axis, pairs)
        low = jnp.where(side == 0, rows, other)
        high = jnp.where(side == 0, other, rows)
        rows = jnp.concatenate([low, high], 0)
    return rows.reshape(-1)[:size].reshape(value.shape).astype(value.dtype)


def weight_grad(padded, delta_field):
    local_grad = kernel_grad(padded, delta_field)
    return tree_sum(local_grad, ("dp", "gy", "gx"))


def per_device(volumes, weight_one, weight_two, cotangent):
    layout = volumes.shape
    depth = layout[4]
    flipped = jnp.transpose(weight_two[::-1], (0, 2, 1))
    rim_input = extended(volumes, (("gx", 1), ("gy", 2)), 1)
    act_one = lax.optimization_barrier(conv_block(rim_input, weight_one))
    hidden = jax.nn.silu(act_one).astype(jnp.bfloat16)
    rim_hidden = extended(hidden, (("gx", 1), ("gy", 2)), 1)
    act_two = conv_block(rim_hidden, weight_two)
    features = jax.nn.silu(act_two).astype(jnp.bfloat16)
    delta_two = (cotangent.astype(jnp.float32) * swish_slope(act_two)).astype(jnp.bfloat16)
    grad_two = weight_grad(rim_hidden, delta_two)
    rim_delta = extended(delta_two, (("gx", 1), ("gy", 2)), 1)
    back_grad = conv_block(rim_delta, flipped)
    delta_one = (back_grad * swish_slope(act_one)).astype(jnp.bfloat16)
    grad_one = weight_grad(rim_input, delta_one)
    return (features, grad_one.reshape(27, depth, depth), grad_two.reshape(27, depth, depth))


def solution(mesh):
    in_specs = (P("dp", "gx", "gy", None, None), P(), P(), P("dp", "gx", "gy", None, None))
    out_specs = (P("dp", "gx", "gy", None, None), P(), P())
    return jax.shard_map(
        per_device, mesh=mesh, in_specs=in_specs, out_specs=out_specs, check_vma=False
    )
```

```python
import jax
import jax.numpy as jnp
from jax import lax
from jax.sharding import PartitionSpec as P


def extended(cells, sides, width):
    for axis, dim in sides:
        count = lax.axis_size(axis)
        ends = count - 1
        head = lax.slice_in_dim(cells, 0, width, axis=dim)
        tail = lax.slice_in_dim(cells, cells.shape[dim] - width, cells.shape[dim], axis=dim)
        cells = jnp.concatenate(
            [
                lax.ppermute(tail, axis, [(i, (i + 1) % count) for i in range(ends)]),
                cells,
                lax.ppermute(head, axis, [((i + 1) % count, i) for i in range(ends)]),
            ],
            axis=dim,
        )
    return cells


def conv_block(padded, kernel):
    depth = kernel.shape[1]
    cube_kernel = kernel.reshape(3, 3, 3, depth, depth)
    return lax.conv_general_dilated(
        padded,
        cube_kernel,
        (1, 1, 1),
        ((0, 0), (0, 0), (1, 1)),
        dimension_numbers=("NDHWC", "DHWIO", "NDHWC"),
        preferred_element_type=jnp.float32,
    )


def kernel_grad(padded, delta_field):
    depth = delta_field.shape[4]
    result = lax.conv_general_dilated(
        padded,
        delta_field,
        (1, 1, 1),
        ((0, 0), (0, 0), (1, 1)),
        dimension_numbers=("CDHWN", "IDHWO", "DHWNC"),
        preferred_element_type=jnp.float32,
    )
    return result.reshape(27 * depth, depth)


def swish_slope(value):
    sigma = jax.nn.sigmoid(value)
    return sigma * (1.0 + value * (1.0 - sigma))


def tree_sum(value, axes):
    sizes = [lax.axis_size(axis) for axis in axes]
    if any(n & (n - 1) for n in sizes):
        return lax.psum(value, axes)
    steps = []
    total = 1
    for axis, n in zip(axes, sizes):
        bit = 1
        while bit < n:
            steps.append((axis, n, bit))
            bit *= 2
        total *= n
    flat = value.reshape(-1)
    unit = total * 8 * 128
    size = flat.shape[0]
    rows = jnp.pad(flat, (0, -(-size // unit) * unit - size)).reshape(-1, 128)
    sides = []
    for axis, n, bit in steps:
        side = (lax.axis_index(axis) // bit) % 2
        half = rows.shape[0] // 2
        pairs = [(i, i ^ bit) for i in range(n)]
        keep = lax.dynamic_slice_in_dim(rows, side * half, half, 0)
        send = lax.dynamic_slice_in_dim(rows, (1 - side) * half, half, 0)
        rows = keep + lax.ppermute(send, axis, pairs)
        sides.append(side)
    rows = rows.astype(jnp.bfloat16)
    for (axis, n, bit), side in zip(reversed(steps), reversed(sides)):
        pairs = [(i, i ^ bit) for i in range(n)]
        other = lax.ppermute(rows, axis, pairs)
        low = jnp.where(side == 0, rows, other)
        high = jnp.where(side == 0, other, rows)
        rows = jnp.concatenate([low, high], 0)
    return rows.reshape(-1)[:size].reshape(value.shape).astype(value.dtype)


def weight_grad(padded, delta_field):
    local_grad = kernel_grad(padded, delta_field)
    return tree_sum(local_grad, ("dp", "gy", "gx"))


def per_device(volumes, weight_one, weight_two, cotangent):
    layout = volumes.shape
    depth = layout[4]
    flipped = jnp.transpose(weight_two[::-1], (0, 2, 1))
    rim_input = extended(volumes, (("gx", 1), ("gy", 2)), 1)
    act_one = lax.optimization_barrier(conv_block(rim_input, weight_one))
    hidden = jax.nn.silu(act_one).astype(jnp.bfloat16)
    rim_hidden = extended(hidden, (("gx", 1), ("gy", 2)), 1)
    act_two = conv_block(rim_hidden, weight_two)
    features = jax.nn.silu(act_two).astype(jnp.bfloat16)
    delta_two = (cotangent.astype(jnp.float32) * swish_slope(act_two)).astype(jnp.bfloat16)
    local_two = kernel_grad(rim_hidden, delta_two)
    rim_delta = extended(delta_two, (("gx", 1), ("gy", 2)), 1)
    back_grad = conv_block(rim_delta, flipped)
    delta_one = (back_grad * swish_slope(act_one)).astype(jnp.bfloat16)
    local_one = kernel_grad(rim_input, delta_one)
    grad_one, grad_two = tree_sum(jnp.stack([local_one, local_two]), ("dp", "gy", "gx"))
    return (features, grad_one.reshape(27, depth, depth), grad_two.reshape(27, depth, depth))


def solution(mesh):
    in_specs = (P("dp", "gx", "gy", None, None), P(), P(), P("dp", "gx", "gy", None, None))
    out_specs = (P("dp", "gx", "gy", None, None), P(), P())
    return jax.shard_map(
        per_device, mesh=mesh, in_specs=in_specs, out_specs=out_specs, check_vma=False
    )
```

```python
import jax
import jax.numpy as jnp
from jax import lax
from jax.sharding import PartitionSpec as P


def extended(cells, sides, width):
    for axis, dim in sides:
        count = lax.axis_size(axis)
        ends = count - 1
        head = lax.slice_in_dim(cells, 0, width, axis=dim)
        tail = lax.slice_in_dim(cells, cells.shape[dim] - width, cells.shape[dim], axis=dim)
        cells = jnp.concatenate(
            [
                lax.ppermute(tail, axis, [(i, (i + 1) % count) for i in range(ends)]),
                cells,
                lax.ppermute(head, axis, [((i + 1) % count, i) for i in range(ends)]),
            ],
            axis=dim,
        )
    return cells


def conv_block(padded, kernel):
    depth = kernel.shape[1]
    cube_kernel = kernel.reshape(3, 3, 3, depth, depth)
    return lax.conv_general_dilated(
        padded,
        cube_kernel,
        (1, 1, 1),
        ((0, 0), (0, 0), (1, 1)),
        dimension_numbers=("NDHWC", "DHWIO", "NDHWC"),
        preferred_element_type=jnp.float32,
    )


def kernel_grad(padded, delta_field):
    depth = delta_field.shape[4]
    result = lax.conv_general_dilated(
        padded,
        delta_field,
        (1, 1, 1),
        ((0, 0), (0, 0), (1, 1)),
        dimension_numbers=("CDHWN", "IDHWO", "DHWNC"),
        preferred_element_type=jnp.float32,
    )
    return result.reshape(27 * depth, depth)


def swish_slope(value):
    sigma = jax.nn.sigmoid(value)
    return sigma * (1.0 + value * (1.0 - sigma))


def tree_sum(value, axes):
    sizes = [lax.axis_size(axis) for axis in axes]
    if any(n & (n - 1) for n in sizes):
        return lax.psum(value, axes)
    steps = []
    total = 1
    for axis, n in zip(axes, sizes):
        bit = 1
        while bit < n:
            steps.append((axis, n, bit))
            bit *= 2
        total *= n
    flat = value.reshape(-1)
    unit = total * 8 * 128
    size = flat.shape[0]
    rows = jnp.pad(flat, (0, -(-size // unit) * unit - size)).reshape(-1, 128)
    sides = []
    for axis, n, bit in steps:
        side = (lax.axis_index(axis) // bit) % 2
        half = rows.shape[0] // 2
        pairs = [(i, i ^ bit) for i in range(n)]
        keep = lax.dynamic_slice_in_dim(rows, side * half, half, 0)
        send = lax.dynamic_slice_in_dim(rows, (1 - side) * half, half, 0)
        rows = keep + lax.ppermute(send, axis, pairs)
        sides.append(side)
    rows = rows.astype(jnp.bfloat16)
    for (axis, n, bit), side in zip(reversed(steps), reversed(sides)):
        pairs = [(i, i ^ bit) for i in range(n)]
        other = lax.ppermute(rows, axis, pairs)
        low = jnp.where(side == 0, rows, other)
        high = jnp.where(side == 0, other, rows)
        rows = jnp.concatenate([low, high], 0)
    return rows.reshape(-1)[:size].reshape(value.shape).astype(value.dtype)


def weight_grad(padded, delta_field):
    local_grad = kernel_grad(padded, delta_field)
    return tree_sum(local_grad, ("dp", "gy", "gx"))


def per_device(volumes, weight_one, weight_two, cotangent):
    layout = volumes.shape
    depth = layout[4]
    flipped = jnp.transpose(weight_two[::-1], (0, 2, 1))
    rim_input = extended(volumes, (("gy", 2), ("gx", 1)), 1)
    act_one = lax.optimization_barrier(conv_block(rim_input, weight_one))
    hidden = jax.nn.silu(act_one).astype(jnp.bfloat16)
    rim_hidden = extended(hidden, (("gy", 2), ("gx", 1)), 1)
    act_two = conv_block(rim_hidden, weight_two)
    features = jax.nn.silu(act_two).astype(jnp.bfloat16)
    delta_two = (cotangent.astype(jnp.float32) * swish_slope(act_two)).astype(jnp.bfloat16)
    grad_two = weight_grad(rim_hidden, delta_two)
    rim_delta = extended(delta_two, (("gy", 2), ("gx", 1)), 1)
    back_grad = conv_block(rim_delta, flipped)
    delta_one = (back_grad * swish_slope(act_one)).astype(jnp.bfloat16)
    grad_one = weight_grad(rim_input, delta_one)
    return (features, grad_one.reshape(27, depth, depth), grad_two.reshape(27, depth, depth))


def solution(mesh):
    in_specs = (P("dp", "gx", "gy", None, None), P(), P(), P("dp", "gx", "gy", None, None))
    out_specs = (P("dp", "gx", "gy", None, None), P(), P())
    return jax.shard_map(
        per_device, mesh=mesh, in_specs=in_specs, out_specs=out_specs, check_vma=False
    )
```
